512 devices in a mesh: lsec: 32 (over x, z), rsec: 16 (over y, core).
Axes of the slice: x: 4, y: 8, z: 8, core: 2. Of those that a mesh axis runs over, the one named last changes fastest.
Arguments:
- psi: bfloat16 [8192, 4096], P('lsec', 'rsec'), may hold values from -8 to 8
- left_env: bfloat16 [12, 8192, 256], P(None, ('lsec', 'rsec')), may hold values from -2 to 2
- right_env: bfloat16 [12, 4096, 256], P(None, 'rsec', 'lsec'), may hold values from -2 to 2
- left_dims: int32 [32], P('lsec'), may hold values from 1 to 256, 6144 in all
- right_dims: int32 [16], P('rsec'), may hold values from 1 to 256, 3072 in all
- term_shift: int32 [12, 2], replicated, may hold values from -1 to 1, as said below
Outputs:
- image_one: bfloat16 [8192, 4096], P('lsec', 'rsec')
- image_two: bfloat16 [8192, 4096], P('lsec', 'rsec')
- projected: float32 [2, 2], replicated
The draws below stay inside these ranges and needn't reach their ends.
Inputs may be any that keep to these rules, and one draw needn't show every extreme that they name: `term_shift`: each term shifts the left and the right sector by -1, 0 or 1; each of the nine pairs of shifts belongs to some term.
All inputs are finite; a program needn't handle non-finite values. No bound on the sum of `left_dims` or of `right_dims` on one device may be relied on, other than what follows from the above.
Results may differ from the reference program's by a relative error of at most 0.0095.
Values may be sent and summed in bfloat16 or wider, within the bound.
No kernel may reach another device: no remote copies, remote signals or barrier semaphores. Data moves between devices by JAX's collectives and lax.ppermute only.
A program may use at most 64 MiB of HBM per device.

```python
import math
import jax
import jax.numpy as jnp
import numpy as np
from jax import lax

DB = 256
W = 12
NL = 32
NR = 16


def draw_term_shift(key, part):
    order = jax.random.permutation(key, W)
    combo = order % 9
    return jnp.stack([combo // 3 - 1, combo % 3 - 1], axis=1).astype(jnp.int32)


def draw_psi(key, part):
    rows = jnp.arange(NL * DB, dtype=jnp.float32) / float(NL * DB - 1)
    base = jnp.clip(jax.random.normal(key, (NL * DB, NR * DB), jnp.float32), -4.0, 4.0)
    amp = jnp.exp(rows * jnp.log(2.0))[:, None] * jnp.ones((1, NR * DB), jnp.float32)
    return (base * amp).astype(jnp.bfloat16)


def env_blocks(key, sectors):
    shape = (W, sectors * DB, DB)
    noise = jnp.clip(jax.random.normal(key, shape, jnp.float32), -4.0, 4.0)
    rows = jnp.arange(sectors * DB, dtype=jnp.int32) % DB
    cols = jnp.arange(DB, dtype=jnp.int32)
    diagonal = (rows[:, None] == cols[None, :]).astype(jnp.float32)
    return (noise * float(DB) ** (-0.5) + diagonal[None, :, :]).astype(jnp.bfloat16)


def draw_left_env(key, part):
    return env_blocks(jax.random.fold_in(key, 11), NL)


def draw_right_env(key, part):
    return env_blocks(jax.random.fold_in(key, 23), NR)


def length_profile(amount, total, most, slope):
    weights = [(1 << 20) // math.isqrt(standing ** slope) + 1 for standing in range(2, amount + 1)]
    spare, counts = total - most - (amount - 1), [1] * (amount - 1)
    while spare > 0:
        free = [i for i in range(amount - 1) if counts[i] < most]
        mass, left = sum([weights[i] for i in free]), spare
        for i in free:
            extra = min(most - counts[i], max(1, left * weights[i] // mass), spare)
            counts[i] = counts[i] + extra
            spare = spare - extra
    return np.array([most] + counts)


def uneven_parts(stream_key, number_of, total, most, slope):
    if number_of == 2:
        one = jax.random.randint(stream_key, (), max(1, total - most), min(most, total - 1) + 1)
        return jnp.stack([one, total - one])
    lengths = jnp.asarray(length_profile(number_of, total, most, slope), jnp.int32)
    pairs = (number_of - 1) // 2
    donor, receiver = lengths[1:1 + 2 * pairs:2], lengths[2:2 + 2 * pairs:2]
    room = jnp.minimum(donor - 1, most - receiver)
    moved = jax.random.randint(jax.random.fold_in(stream_key, 1), (pairs,), 0, 1 << 20) % (room + 1)
    lengths = lengths.at[1:1 + 2 * pairs:2].set(donor - moved).at[2:2 + 2 * pairs:2].set(receiver + moved)
    return lengths[jax.random.permutation(jax.random.fold_in(stream_key, 2), number_of)]


def setup_inputs(seed: int = 0) -> dict:
    seeds = jax.random.split(jax.random.key(seed), 7)
    return {
        "psi": draw_psi(jax.random.fold_in(seeds[6], 71), 0),
        "left_env": draw_left_env(jax.random.fold_in(seeds[6], 71), 0),
        "right_env": draw_right_env(jax.random.fold_in(seeds[6], 71), 0),
        "left_dims": uneven_parts(seeds[3], NL, NL * DB * 3 // 4, DB, 2).astype(jnp.int32),
        "right_dims": uneven_parts(seeds[4], NR, NR * DB * 3 // 4, DB, 2).astype(jnp.int32),
        "term_shift": draw_term_shift(jax.random.fold_in(seeds[6], 71), 0),
    }


def live_mask(left_dims, right_dims):
    rows = jnp.arange(NL * DB, dtype=jnp.int32)
    cols = jnp.arange(NR * DB, dtype=jnp.int32)
    row_live = rows % DB < left_dims[rows // DB]
    col_live = cols % DB < right_dims[cols // DB]
    return row_live[:, None] & col_live[None, :]

def apply_terms(vector, left_env, right_env, term_shift, mask):
    blocks = vector.reshape(NL, DB, NR, DB)
    padded = jnp.pad(blocks, ((1, 1), (0, 0), (1, 1), (0, 0)))
    total = jnp.zeros((NL, DB, NR, DB), jnp.float32)
    zero = jnp.zeros((), jnp.int32)
    for term in range(W):
        start_left = (1 - term_shift[term, 0]).astype(jnp.int32)
        start_right = (1 - term_shift[term, 1]).astype(jnp.int32)
        source = lax.dynamic_slice(padded, (start_left, zero, start_right, zero), (NL, DB, NR, DB))
        left_blocks = left_env[term].reshape(NL, DB, DB).astype(jnp.float32)
        inner = jnp.einsum('aik,akbj->aibj', left_blocks, source.astype(jnp.float32)).astype(jnp.bfloat16)
        inner = lax.optimization_barrier(inner)
        right_blocks = right_env[term].reshape(NR, DB, DB).astype(jnp.float32)
        total = total + jnp.einsum('aibj,bjn->aibn', inner.astype(jnp.float32), right_blocks)
    return total.reshape(NL * DB, NR * DB) * mask.astype(jnp.float32)

def reference(psi, left_env, right_env, left_dims, right_dims, term_shift):
    mask = live_mask(left_dims, right_dims)
    live = jnp.where(mask, psi, jnp.zeros_like(psi))
    count = float(NL * NR * DB * DB)
    live32 = live.astype(jnp.float32)
    total_sq = jnp.sum(live32 * live32)
    first = (live32 * lax.rsqrt(total_sq / count + 1e-06)).astype(jnp.bfloat16)
    image1 = apply_terms(first, left_env, right_env, term_shift, mask)
    first32 = first.astype(jnp.float32)
    alpha = jnp.sum(first32 * image1) / count
    rest = image1 - alpha * first32
    rest_sq = jnp.sum(rest * rest) / count
    second = (rest * lax.rsqrt(rest_sq + 1e-06)).astype(jnp.bfloat16)
    image2 = apply_terms(second, left_env, right_env, term_shift, mask)
    second32 = second.astype(jnp.float32)
    upper = jnp.sum(first32 * image2) / count
    lower = jnp.sum(second32 * image1) / count
    corner = jnp.sum(second32 * image2) / count
    projected = jnp.stack([jnp.stack([alpha, upper]), jnp.stack([lower, corner])])
    return (image1.astype(jnp.bfloat16), image2.astype(jnp.bfloat16), projected)
```

```python
import jax
import jax.numpy as jnp
from jax import lax
from jax.sharding import PartitionSpec as P

AXES = ("lsec", "rsec")


def extended(array, sides, width):
    for axis, dim in sides:
        devices, length = (lax.axis_size(axis), array.shape[dim])
        up = [(i, (i + 1) % devices) for i in range(devices - 1)]
        down = [(j, i) for i, j in up]
        last = lax.slice_in_dim(array, length - width, length, axis=dim)
        leading = lax.slice_in_dim(array, 0, width, axis=dim)
        before = lax.ppermute(last, axis, up)
        after = lax.ppermute(leading, axis, down)
        array = jnp.concatenate([before, array, after], axis=dim)
    return array


def halo(block):
    width = block.shape[0]
    return extended(block.reshape(1, width, 1, width), (("lsec", 0), ("rsec", 2)), 1)


def total(parts):
    devices = lax.axis_size(AXES)
    spread = jnp.broadcast_to(parts[None, :], (devices, parts.shape[0]))
    gathered = lax.all_to_all(spread, AXES, 0, 0, tiled=True)
    return jnp.sum(gathered, axis=0)


def apply_terms(grid, left_env, right_env, term_shift, mask):
    width = grid.shape[1]
    zero = jnp.zeros((), jnp.int32)

    def pick(shift):
        start_left = 1 - shift[0]
        start_right = 1 - shift[1]
        return lax.dynamic_slice(
            grid, (start_left, zero, start_right, zero), (1, width, 1, width)
        ).reshape(width, width)

    sources = jax.vmap(pick)(term_shift)
    inner = jnp.einsum(
        "wik,wkj->wij", left_env, sources, preferred_element_type=jnp.float32
    ).astype(jnp.bfloat16)
    total_ = jnp.einsum(
        "wij,wjn->in", inner, right_env, preferred_element_type=jnp.float32
    )
    return total_ * mask


def on_device(psi, left_env, right_env, left_dims, right_dims, term_shift):
    width = psi.shape[0]
    offsets = jnp.arange(width, dtype=jnp.int32)
    mask_bool = (offsets < left_dims[0])[:, None] & (offsets < right_dims[0])[None, :]
    mask = mask_bool.astype(jnp.float32)
    count = float(lax.axis_size("lsec") * lax.axis_size("rsec") * width * width)
    left_full = lax.all_gather(left_env, "rsec", axis=1, tiled=True)
    right_full = lax.all_gather(right_env, "lsec", axis=2, tiled=True)

    live = jnp.where(mask_bool, psi, jnp.zeros_like(psi))
    live_grid = halo(live)
    live32 = live.astype(jnp.float32)
    total_sq = total(jnp.sum(live32 * live32)[None])[0]
    scale1 = lax.rsqrt(total_sq / count + 1e-06)
    first_grid = (live_grid.astype(jnp.float32) * scale1).astype(jnp.bfloat16)
    first = first_grid[1, :, 1, :]
    image1 = apply_terms(first_grid, left_full, right_full, term_shift, mask)

    image1_grid = halo(image1)
    first32 = first.astype(jnp.float32)
    alpha = total(jnp.sum(first32 * image1)[None])[0] / count
    rest = image1 - alpha * first32
    rest_sq = total(jnp.sum(rest * rest)[None])[0] / count
    scale2 = lax.rsqrt(rest_sq + 1e-06)
    rest_grid = image1_grid - alpha * first_grid.astype(jnp.float32)
    second_grid = (rest_grid * scale2).astype(jnp.bfloat16)
    second = second_grid[1, :, 1, :]
    image2 = apply_terms(second_grid, left_full, right_full, term_shift, mask)

    second32 = second.astype(jnp.float32)
    sums = total(
        jnp.stack(
            [jnp.sum(first32 * image2), jnp.sum(second32 * image1), jnp.sum(second32 * image2)]
        )
    )
    projected = jnp.stack(
        [jnp.stack([alpha, sums[0] / count]), jnp.stack([sums[1] / count, sums[2] / count])]
    )
    return (image1.astype(jnp.bfloat16), image2.astype(jnp.bfloat16), projected)


def solution(mesh):
    in_specs = (
        P("lsec", "rsec"),
        P(None, ("lsec", "rsec"), None),
        P(None, "rsec", "lsec"),
        P("lsec"),
        P("rsec"),
        P(),
    )
    out_specs = (P("lsec", "rsec"), P("lsec", "rsec"), P())
    return jax.shard_map(
        on_device, mesh=mesh, in_specs=in_specs, out_specs=out_specs, check_vma=False
    )
```

```python
import jax
import jax.numpy as jnp
from jax import lax
from jax.sharding import PartitionSpec as P

AXES = ("lsec", "rsec")


def extended(array, sides, width):
    for axis, dim in sides:
        devices, length = (lax.axis_size(axis), array.shape[dim])
        up = [(i, (i + 1) % devices) for i in range(devices - 1)]
        down = [(j, i) for i, j in up]
        last = lax.slice_in_dim(array, length - width, length, axis=dim)
        leading = lax.slice_in_dim(array, 0, width, axis=dim)
        before = lax.ppermute(last, axis, up)
        after = lax.ppermute(leading, axis, down)
        array = jnp.concatenate([before, array, after], axis=dim)
    return array


def halo(block):
    width = block.shape[0]
    return extended(block.reshape(1, width, 1, width), (("lsec", 0), ("rsec", 2)), 1)


def total(parts):
    devices = lax.axis_size(AXES)
    spread = jnp.broadcast_to(parts[None, :], (devices, parts.shape[0]))
    gathered = lax.all_to_all(spread, AXES, 0, 0, tiled=True)
    return jnp.sum(gathered, axis=0)


def split(x):
    high = x.astype(jnp.bfloat16)
    low = (x - high.astype(jnp.float32)).astype(jnp.bfloat16)
    return high, low


def apply_terms(grid, left_env, right_env, term_shift, mask):
    width = grid.shape[1]
    zero = jnp.zeros((), jnp.int32)

    def pick(shift):
        start_left = 1 - shift[0]
        start_right = 1 - shift[1]
        return lax.dynamic_slice(
            grid, (start_left, zero, start_right, zero), (1, width, 1, width)
        ).reshape(width, width)

    sources = jax.vmap(pick)(term_shift)

    def left(src):
        return jnp.einsum("iwk,wkj->wij", left_env, src, preferred_element_type=jnp.float32)

    if sources.dtype == jnp.bfloat16:
        inner = left(sources)
    else:
        high, low = split(sources)
        inner = left(high) + left(low)

    def right(part):
        return jnp.einsum("wij,nwj->in", part, right_env, preferred_element_type=jnp.float32)

    high, low = split(inner)
    return (right(high) + right(low)) * mask


def on_device(psi, left_env, right_env, left_dims, right_dims, term_shift):
    width = psi.shape[0]
    offsets = jnp.arange(width, dtype=jnp.int32)
    mask_bool = (offsets < left_dims[0])[:, None] & (offsets < right_dims[0])[None, :]
    mask = mask_bool.astype(jnp.float32)
    count = float(lax.axis_size("lsec") * lax.axis_size("rsec") * width * width)
    left_full = lax.all_gather(jnp.transpose(left_env, (1, 0, 2)), "rsec", axis=0, tiled=True)
    right_full = lax.all_gather(jnp.transpose(right_env, (2, 0, 1)), "lsec", axis=0, tiled=True)

    live = jnp.where(mask_bool, psi, jnp.zeros_like(psi))
    live_grid = halo(live)
    h1 = apply_terms(live_grid, left_full, right_full, term_shift, mask)
    h1_grid = halo(h1)
    hh1 = apply_terms(h1_grid, left_full, right_full, term_shift, mask)

    live32 = live.astype(jnp.float32)
    first_sums = total(jnp.stack([jnp.sum(live32 * live32), jnp.sum(live32 * h1)]))
    scale1 = lax.rsqrt(first_sums[0] / count + 1e-06)
    scale1_sq = scale1 * scale1
    alpha = scale1_sq * first_sums[1] / count

    r = h1 - alpha * live32
    g = hh1 - alpha * h1
    second_sums = total(
        jnp.stack([jnp.sum(r * r), jnp.sum(live32 * g), jnp.sum(r * h1), jnp.sum(r * g)])
    )
    scale2 = lax.rsqrt(scale1_sq * second_sums[0] / count + 1e-06)
    both = scale1 * scale2
    upper = scale1_sq * scale2 * second_sums[1] / count
    lower = scale1_sq * scale2 * second_sums[2] / count
    corner = both * both * second_sums[3] / count
    projected = jnp.stack([jnp.stack([alpha, upper]), jnp.stack([lower, corner])])
    image1 = (h1 * scale1).astype(jnp.bfloat16)
    image2 = (g * both).astype(jnp.bfloat16)
    return (image1, image2, projected)


def solution(mesh):
    in_specs = (
        P("lsec", "rsec"),
        P(None, ("lsec", "rsec"), None),
        P(None, "rsec", "lsec"),
        P("lsec"),
        P("rsec"),
        P(),
    )
    out_specs = (P("lsec", "rsec"), P("lsec", "rsec"), P())
    return jax.shard_map(
        on_device, mesh=mesh, in_specs=in_specs, out_specs=out_specs, check_vma=False
    )
```

```python
import jax
import jax.numpy as jnp
from jax import lax
from jax.sharding import PartitionSpec as P

AXES = ("lsec", "rsec")


def extended(array, sides, width):
    for axis, dim in sides:
        devices, length = (lax.axis_size(axis), array.shape[dim])
        up = [(i, (i + 1) % devices) for i in range(devices - 1)]
        down = [(j, i) for i, j in up]
        last = lax.slice_in_dim(array, length - width, length, axis=dim)
        leading = lax.slice_in_dim(array, 0, width, axis=dim)
        before = lax.ppermute(last, axis, up)
        after = lax.ppermute(leading, axis, down)
        array = jnp.concatenate([before, array, after], axis=dim)
    return array


def halo(block):
    width = block.shape[0]
    return extended(block.reshape(1, width, 1, width), (("lsec", 0), ("rsec", 2)), 1)


def total(parts):
    devices = lax.axis_size(AXES)
    spread = jnp.broadcast_to(parts[None, :], (devices, parts.shape[0]))
    gathered = lax.all_to_all(spread, AXES, 0, 0, tiled=True)
    return jnp.sum(gathered, axis=0)


def gathered(block, axis):
    devices = lax.axis_size(axis)
    spread = lax.optimization_barrier(jnp.broadcast_to(block[None], (devices,) + block.shape))
    out = lax.all_to_all(spread, axis, 0, 0, tiled=True)
    return out.reshape((devices * block.shape[0],) + block.shape[1:])


def split(x):
    high = x.astype(jnp.bfloat16)
    low = (x - high.astype(jnp.float32)).astype(jnp.bfloat16)
    return high, low


def apply_terms(grid, left_env, right_env, term_shift, mask):
    width = grid.shape[1]
    zero = jnp.zeros((), jnp.int32)

    def pick(shift):
        start_left = 1 - shift[0]
        start_right = 1 - shift[1]
        return lax.dynamic_slice(
            grid, (start_left, zero, start_right, zero), (1, width, 1, width)
        ).reshape(width, width)

    sources = jax.vmap(pick)(term_shift)

    def left(src):
        return jnp.einsum("iwk,wkj->wij", left_env, src, preferred_element_type=jnp.float32)

    if sources.dtype == jnp.bfloat16:
        inner = left(sources)
    else:
        high, low = split(sources)
        inner = left(high) + left(low)

    def right(part):
        return jnp.einsum("wij,nwj->in", part, right_env, preferred_element_type=jnp.float32)

    high, low = split(inner)
    return (right(high) + right(low)) * mask


def on_device(psi, left_env, right_env, left_dims, right_dims, term_shift):
    width = psi.shape[0]
    offsets = jnp.arange(width, dtype=jnp.int32)
    mask_bool = (offsets < left_dims[0])[:, None] & (offsets < right_dims[0])[None, :]
    mask = mask_bool.astype(jnp.float32)
    count = float(lax.axis_size("lsec") * lax.axis_size("rsec") * width * width)
    left_full = lax.all_gather(jnp.transpose(left_env, (1, 0, 2)), "rsec", axis=0, tiled=True)
    right_full = gathered(jnp.transpose(right_env, (2, 0, 1)), "lsec")

    live = jnp.where(mask_bool, psi, jnp.zeros_like(psi))
    live_grid = halo(live)
    h1 = apply_terms(live_grid, left_full, right_full, term_shift, mask)
    h1_grid = halo(h1)
    hh1 = apply_terms(h1_grid, left_full, right_full, term_shift, mask)

    live32 = live.astype(jnp.float32)
    first_sums = total(jnp.stack([jnp.sum(live32 * live32), jnp.sum(live32 * h1)]))
    scale1 = lax.rsqrt(first_sums[0] / count + 1e-06)
    scale1_sq = scale1 * scale1
    alpha = scale1_sq * first_sums[1] / count

    r = h1 - alpha * live32
    g = hh1 - alpha * h1
    second_sums = total(
        jnp.stack([jnp.sum(r * r), jnp.sum(live32 * g), jnp.sum(r * h1), jnp.sum(r * g)])
    )
    scale2 = lax.rsqrt(scale1_sq * second_sums[0] / count + 1e-06)
    both = scale1 * scale2
    upper = scale1_sq * scale2 * second_sums[1] / count
    lower = scale1_sq * scale2 * second_sums[2] / count
    corner = both * both * second_sums[3] / count
    projected = jnp.stack([jnp.stack([alpha, upper]), jnp.stack([lower, corner])])
    image1 = (h1 * scale1).astype(jnp.bfloat16)
    image2 = (g * both).astype(jnp.bfloat16)
    return (image1, image2, projected)


def solution(mesh):
    in_specs = (
        P("lsec", "rsec"),
        P(None, ("lsec", "rsec"), None),
        P(None, "rsec", "lsec"),
        P("lsec"),
        P("rsec"),
        P(),
    )
    out_specs = (P("lsec", "rsec"), P("lsec", "rsec"), P())
    return jax.shard_map(
        on_device, mesh=mesh, in_specs=in_specs, out_specs=out_specs, check_vma=False
    )
```

```python
import jax
import jax.numpy as jnp
from jax import lax
from jax.sharding import PartitionSpec as P

AXES = ("lsec", "rsec")


def extended(array, sides, width):
    for axis, dim in sides:
        devices, length = (lax.axis_size(axis), array.shape[dim])
        up = [(i, (i + 1) % devices) for i in range(devices - 1)]
        down = [(j, i) for i, j in up]
        last = lax.slice_in_dim(array, length - width, length, axis=dim)
        leading = lax.slice_in_dim(array, 0, width, axis=dim)
        before = lax.ppermute(last, axis, up)
        after = lax.ppermute(leading, axis, down)
        array = jnp.concatenate([before, array, after], axis=dim)
    return array


def halo(block):
    width = block.shape[0]
    return extended(block.reshape(1, width, 1, width), (("lsec", 0), ("rsec", 2)), 1)


def total(parts):
    devices = lax.axis_size(AXES)
    spread = jnp.broadcast_to(parts[None, :], (devices, parts.shape[0]))
    gathered = lax.all_to_all(spread, AXES, 0, 0, tiled=True)
    return jnp.sum(gathered, axis=0)


def gathered(block, axis):
    devices = lax.axis_size(axis)
    spread = lax.optimization_barrier(jnp.broadcast_to(block[None], (devices,) + block.shape))
    out = lax.all_to_all(spread, axis, 0, 0, tiled=True)
    return out.reshape((devices * block.shape[0],) + block.shape[1:])


def split(x):
    high = x.astype(jnp.bfloat16)
    low = (x - high.astype(jnp.float32)).astype(jnp.bfloat16)
    return high, low


def apply_terms(grid, left_env, right_env, term_shift, mask):
    width = grid.shape[1]
    zero = jnp.zeros((), jnp.int32)

    def pick(shift):
        start_left = 1 - shift[0]
        start_right = 1 - shift[1]
        return lax.dynamic_slice(
            grid, (start_left, zero, start_right, zero), (1, width, 1, width)
        ).reshape(width, width)

    sources = jax.vmap(pick)(term_shift)

    def left(src):
        return jnp.einsum("iwk,wkj->wij", left_env, src, preferred_element_type=jnp.float32)

    if sources.dtype == jnp.bfloat16:
        inner = left(sources)
    else:
        high, low = split(sources)
        inner = left(high) + left(low)

    def right(part):
        return jnp.einsum("wij,nwj->in", part, right_env, preferred_element_type=jnp.float32)

    high, low = split(inner)
    return (right(high) + right(low)) * mask


def on_device(psi, left_env, right_env, left_dims, right_dims, term_shift):
    width = psi.shape[0]
    offsets = jnp.arange(width, dtype=jnp.int32)
    mask_bool = (offsets < left_dims[0])[:, None] & (offsets < right_dims[0])[None, :]
    mask = mask_bool.astype(jnp.float32)
    count = float(lax.axis_size("lsec") * lax.axis_size("rsec") * width * width)
    left_full = lax.all_gather(jnp.transpose(left_env, (1, 0, 2)), "rsec", axis=0, tiled=True)
    right_full = gathered(jnp.transpose(right_env, (2, 0, 1)), "lsec")

    live = jnp.where(mask_bool, psi, jnp.zeros_like(psi))
    live_grid = halo(live)
    h1 = apply_terms(live_grid, left_full, right_full, term_shift, mask)
    h1_grid = halo(h1)
    hh1 = apply_terms(h1_grid, left_full, right_full, term_shift, mask)

    live32 = live.astype(jnp.float32)
    sums = total(
        jnp.stack(
            [
                jnp.sum(h1 * h1),
                jnp.sum(live32 * h1),
                jnp.sum(live32 * live32),
                jnp.sum(live32 * hh1),
                jnp.sum(h1 * hh1),
            ]
        )
    )
    a, b, c, d, e = (sums[i] for i in range(5))
    scale1 = lax.rsqrt(c / count + 1e-06)
    scale1_sq = scale1 * scale1
    alpha = scale1_sq * b / count
    rest_sq = jnp.maximum(scale1_sq * (a - 2.0 * alpha * b + alpha * alpha * c) / count, 0.0)
    scale2 = lax.rsqrt(rest_sq + 1e-06)
    both = scale1 * scale2
    upper = scale1_sq * scale2 * (d - alpha * b) / count
    lower = scale1_sq * scale2 * (a - alpha * b) / count
    corner = both * both * (e - alpha * a - alpha * d + alpha * alpha * b) / count
    projected = jnp.stack([jnp.stack([alpha, upper]), jnp.stack([lower, corner])])
    image1 = (h1 * scale1).astype(jnp.bfloat16)
    image2 = ((hh1 - alpha * h1) * both).astype(jnp.bfloat16)
    return (image1, image2, projected)


def solution(mesh):
    in_specs = (
        P("lsec", "rsec"),
        P(None, ("lsec", "rsec"), None),
        P(None, "rsec", "lsec"),
        P("lsec"),
        P("rsec"),
        P(),
    )
    out_specs = (P("lsec", "rsec"), P("lsec", "rsec"), P())
    return jax.shard_map(
        on_device, mesh=mesh, in_specs=in_specs, out_specs=out_specs, check_vma=False
    )
```

```python
import jax
import jax.numpy as jnp
from jax import lax
from jax.sharding import PartitionSpec as P

AXES = ("lsec", "rsec")


def extended(array, sides, width):
    for axis, dim in sides:
        devices, length = (lax.axis_size(axis), array.shape[dim])
        up = [(i, (i + 1) % devices) for i in range(devices - 1)]
        down = [(j, i) for i, j in up]
        last = lax.slice_in_dim(array, length - width, length, axis=dim)
        leading = lax.slice_in_dim(array, 0, width, axis=dim)
        before = lax.ppermute(last, axis, up)
        after = lax.ppermute(leading, axis, down)
        array = jnp.concatenate([before, array, after], axis=dim)
    return array


def halo(block):
    width = block.shape[0]
    return extended(block.reshape(1, width, 1, width), (("lsec", 0), ("rsec", 2)), 1)


def total(parts):
    devices = lax.axis_size(AXES)
    spread = jnp.broadcast_to(parts[None, :], (devices, parts.shape[0]))
    gathered = lax.all_to_all(spread, AXES, 0, 0, tiled=True)
    return jnp.sum(gathered, axis=0)


def gathered(block, axis):
    devices = lax.axis_size(axis)
    spread = lax.optimization_barrier(jnp.broadcast_to(block[None], (devices,) + block.shape))
    out = lax.all_to_all(spread, axis, 0, 0, tiled=True)
    return out.reshape((devices * block.shape[0],) + block.shape[1:])


def split(x):
    high = x.astype(jnp.bfloat16)
    low = (x - high.astype(jnp.float32)).astype(jnp.bfloat16)
    return high, low


def apply_terms(grid, left_env, right_env, term_shift, mask):
    width = grid.shape[1]
    zero = jnp.zeros((), jnp.int32)

    def pick(shift):
        start_left = 1 - shift[0]
        start_right = 1 - shift[1]
        return lax.dynamic_slice(
            grid, (start_left, zero, start_right, zero), (1, width, 1, width)
        ).reshape(width, width)

    sources = jax.vmap(pick)(term_shift)

    def left(src):
        return jnp.einsum("iwk,wkj->wij", left_env, src, preferred_element_type=jnp.float32)

    if sources.dtype == jnp.bfloat16:
        inner = left(sources)
    else:
        high, low = split(sources)
        inner = left(high) + left(low)

    def right(part):
        return jnp.einsum("wij,nwj->in", part, right_env, preferred_element_type=jnp.float32)

    high, low = split(inner)
    return (right(high) + right(low)) * mask


def on_device(psi, left_env, right_env, left_dims, right_dims, term_shift):
    width = psi.shape[0]
    offsets = jnp.arange(width, dtype=jnp.int32)
    mask_bool = (offsets < left_dims[0])[:, None] & (offsets < right_dims[0])[None, :]
    mask = mask_bool.astype(jnp.float32)
    count = float(lax.axis_size("lsec") * lax.axis_size("rsec") * width * width)
    left_full = lax.all_gather(jnp.transpose(left_env, (1, 0, 2)), "rsec", axis=0, tiled=True)
    right_full = gathered(jnp.transpose(right_env, (2, 0, 1)), "lsec")

    live = jnp.where(mask_bool, psi, jnp.zeros_like(psi))
    live_grid = halo(live)
    h1 = apply_terms(live_grid, left_full, right_full, term_shift, mask)
    h1_grid = halo(h1)
    hh1 = apply_terms(h1_grid, left_full, right_full, term_shift, mask)

    live32 = live.astype(jnp.float32)
    products = jnp.stack([h1 * h1, live32 * h1, live32 * live32, live32 * hh1, h1 * hh1])
    sums = total(jnp.sum(products, axis=(1, 2)))
    a, b, c, d, e = (sums[i : i + 1] for i in range(5))
    scale1 = lax.rsqrt(c / count + 1e-06)
    scale1_sq = scale1 * scale1
    alpha = scale1_sq * b / count
    rest_sq = jnp.maximum(scale1_sq * (a - 2.0 * alpha * b + alpha * alpha * c) / count, 0.0)
    scale2 = lax.rsqrt(rest_sq + 1e-06)
    both = scale1 * scale2
    upper = scale1_sq * scale2 * (d - alpha * b) / count
    lower = scale1_sq * scale2 * (a - alpha * b) / count
    corner = both * both * (e - alpha * a - alpha * d + alpha * alpha * b) / count
    projected = jnp.concatenate([alpha, upper, lower, corner]).reshape(2, 2)
    image1 = (h1 * scale1).astype(jnp.bfloat16)
    image2 = ((hh1 - alpha * h1) * both).astype(jnp.bfloat16)
    return (image1, image2, projected)


def solution(mesh):
    in_specs = (
        P("lsec", "rsec"),
        P(None, ("lsec", "rsec"), None),
        P(None, "rsec", "lsec"),
        P("lsec"),
        P("rsec"),
        P(),
    )
    out_specs = (P("lsec", "rsec"), P("lsec", "rsec"), P())
    return jax.shard_map(
        on_device, mesh=mesh, in_specs=in_specs, out_specs=out_specs, check_vma=False
    )
```

```python
import functools

import jax
import jax.numpy as jnp
from jax import lax
from jax.experimental import pallas as pl
from jax.sharding import PartitionSpec as P

AXES = ("lsec", "rsec")


def extended(array, sides, width):
    for axis, dim in sides:
        devices, length = (lax.axis_size(axis), array.shape[dim])
        up = [(i, (i + 1) % devices) for i in range(devices - 1)]
        down = [(j, i) for i, j in up]
        last = lax.slice_in_dim(array, length - width, length, axis=dim)
        leading = lax.slice_in_dim(array, 0, width, axis=dim)
        before = lax.ppermute(last, axis, up)
        after = lax.ppermute(leading, axis, down)
        array = jnp.concatenate([before, array, after], axis=dim)
    return array


def halo(block):
    width = block.shape[0]
    return extended(block.reshape(1, width, 1, width), (("lsec", 0), ("rsec", 2)), 1)


def total(parts):
    devices = lax.axis_size(AXES)
    spread = jnp.broadcast_to(parts[None, :], (devices, parts.shape[0]))
    gathered = lax.all_to_all(spread, AXES, 0, 0, tiled=True)
    return jnp.sum(gathered, axis=0)


def gathered(block, axis):
    devices = lax.axis_size(axis)
    spread = lax.optimization_barrier(jnp.broadcast_to(block[None], (devices,) + block.shape))
    out = lax.all_to_all(spread, axis, 0, 0, tiled=True)
    return out.reshape((devices * block.shape[0],) + block.shape[1:])


def split(x):
    high = x.astype(jnp.bfloat16)
    low = (x - high.astype(jnp.float32)).astype(jnp.bfloat16)
    return high, low


def apply_terms(grid, left_env, right_env, term_shift, mask):
    width = grid.shape[1]
    zero = jnp.zeros((), jnp.int32)

    def pick(shift):
        start_left = 1 - shift[0]
        start_right = 1 - shift[1]
        return lax.dynamic_slice(
            grid, (start_left, zero, start_right, zero), (1, width, 1, width)
        ).reshape(width, width)

    sources = jax.vmap(pick)(term_shift)

    def left(src):
        return jnp.einsum("iwk,wkj->wij", left_env, src, preferred_element_type=jnp.float32)

    if sources.dtype == jnp.bfloat16:
        inner = left(sources)
    else:
        high, low = split(sources)
        inner = left(high) + left(low)

    def right(part):
        return jnp.einsum("wij,nwj->in", part, right_env, preferred_element_type=jnp.float32)

    high, low = split(inner)
    return (right(high) + right(low)) * mask


def tail_kernel(count, sums_ref, h1_ref, hh1_ref, image1_ref, image2_ref, projected_ref):
    rows = sums_ref[...]
    a, b, c, d, e = (rows[i : i + 1, :] for i in range(5))
    scale1 = lax.rsqrt(c / count + 1e-06)
    scale1_sq = scale1 * scale1
    alpha = scale1_sq * b / count
    rest_sq = jnp.maximum(scale1_sq * (a - 2.0 * alpha * b + alpha * alpha * c) / count, 0.0)
    scale2 = lax.rsqrt(rest_sq + 1e-06)
    both = scale1 * scale2
    upper = scale1_sq * scale2 * (d - alpha * b) / count
    lower = scale1_sq * scale2 * (a - alpha * b) / count
    corner = both * both * (e - alpha * a - alpha * d + alpha * alpha * b) / count
    projected_ref[...] = jnp.concatenate([alpha, upper, lower, corner, rows[4:8, :] * 0.0], axis=0)
    lanes = h1_ref.shape[1] // rows.shape[1]

    def wide(v):
        return jnp.concatenate([v] * lanes, axis=1)

    h1 = h1_ref[...]
    image1_ref[...] = (h1 * wide(scale1)).astype(image1_ref.dtype)
    image2_ref[...] = ((hh1_ref[...] - wide(alpha) * h1) * wide(both)).astype(image2_ref.dtype)


def on_device(psi, left_env, right_env, left_dims, right_dims, term_shift):
    width = psi.shape[0]
    offsets = jnp.arange(width, dtype=jnp.int32)
    mask_bool = (offsets < left_dims[0])[:, None] & (offsets < right_dims[0])[None, :]
    mask = mask_bool.astype(jnp.float32)
    count = float(lax.axis_size("lsec") * lax.axis_size("rsec") * width * width)
    left_full = lax.all_gather(jnp.transpose(left_env, (1, 0, 2)), "rsec", axis=0, tiled=True)
    right_full = gathered(jnp.transpose(right_env, (2, 0, 1)), "lsec")

    live = jnp.where(mask_bool, psi, jnp.zeros_like(psi))
    live_grid = halo(live)
    h1 = apply_terms(live_grid, left_full, right_full, term_shift, mask)
    h1_grid = halo(h1)
    hh1 = apply_terms(h1_grid, left_full, right_full, term_shift, mask)

    live32 = live.astype(jnp.float32)
    products = jnp.stack([h1 * h1, live32 * h1, live32 * live32, live32 * hh1, h1 * hh1])
    sums = total(jnp.sum(products, axis=(1, 2)))
    rows = jnp.broadcast_to(jnp.pad(sums, (0, 3))[:, None], (8, 128))
    image1, image2, projected_rows = pl.pallas_call(
        functools.partial(tail_kernel, count),
        out_shape=(
            jax.ShapeDtypeStruct(h1.shape, jnp.bfloat16),
            jax.ShapeDtypeStruct(h1.shape, jnp.bfloat16),
            jax.ShapeDtypeStruct((8, 128), jnp.float32),
        ),
    )(rows, h1, hh1)
    projected = projected_rows[:4, 0].reshape(2, 2)
    return (image1, image2, projected)


def solution(mesh):
    in_specs = (
        P("lsec", "rsec"),
        P(None, ("lsec", "rsec"), None),
        P(None, "rsec", "lsec"),
        P("lsec"),
        P("rsec"),
        P(),
    )
    out_specs = (P("lsec", "rsec"), P("lsec", "rsec"), P())
    return jax.shard_map(
        on_device, mesh=mesh, in_specs=in_specs, out_specs=out_specs, check_vma=False
    )
```

```python
import functools

import jax
import jax.numpy as jnp
from jax import lax
from jax.experimental import pallas as pl
from jax.experimental.pallas import tpu as pltpu
from jax.sharding import PartitionSpec as P

AXES = ("lsec", "rsec")


def extended(array, sides, width):
    for axis, dim in sides:
        devices, length = (lax.axis_size(axis), array.shape[dim])
        up = [(i, (i + 1) % devices) for i in range(devices - 1)]
        down = [(j, i) for i, j in up]
        last = lax.slice_in_dim(array, length - width, length, axis=dim)
        leading = lax.slice_in_dim(array, 0, width, axis=dim)
        before = lax.ppermute(last, axis, up)
        after = lax.ppermute(leading, axis, down)
        array = jnp.concatenate([before, array, after], axis=dim)
    return array


def halo(block):
    width = block.shape[0]
    return extended(block.reshape(1, 1, width, width), (("lsec", 0), ("rsec", 1)), 1)


def total(parts):
    devices = lax.axis_size(AXES)
    spread = jnp.broadcast_to(parts[None, :], (devices, parts.shape[0]))
    gathered = lax.all_to_all(spread, AXES, 0, 0, tiled=True)
    return jnp.sum(gathered, axis=0)


def gathered(block, axis):
    devices = lax.axis_size(axis)
    spread = lax.optimization_barrier(jnp.broadcast_to(block[None], (devices,) + block.shape))
    out = lax.all_to_all(spread, axis, 0, 0, tiled=True)
    return out.reshape((devices * block.shape[0],) + block.shape[1:])


def split(x):
    high = x.astype(jnp.bfloat16)
    low = (x - high.astype(jnp.float32)).astype(jnp.bfloat16)
    return high, low


def apply_kernel(shift_ref, grid_ref, left_ref, right_ref, mask_ref, out_ref):
    def dot(x, y):
        return jnp.dot(x, y, preferred_element_type=jnp.float32)

    total_ = jnp.zeros(out_ref.shape, jnp.float32)
    for term in range(left_ref.shape[0]):
        source = grid_ref[1 - shift_ref[term, 0], 1 - shift_ref[term, 1]]
        left = left_ref[term]
        if source.dtype == jnp.bfloat16:
            inner = dot(left, source)
        else:
            high, low = split(source)
            inner = dot(left, high) + dot(left, low)
        high, low = split(inner)
        right = right_ref[term]
        total_ = total_ + (dot(high, right) + dot(low, right))
    out_ref[...] = total_ * mask_ref[...]


def apply_terms(grid, left_env, right_env, term_shift, mask):
    vmem = pl.BlockSpec(memory_space=pltpu.VMEM)
    return pl.pallas_call(
        apply_kernel,
        out_shape=jax.ShapeDtypeStruct(mask.shape, jnp.float32),
        in_specs=[pl.BlockSpec(memory_space=pltpu.SMEM), vmem, vmem, vmem, vmem],
        out_specs=vmem,
    )(term_shift, grid, left_env, right_env, mask)


def tail_kernel(count, sums_ref, h1_ref, hh1_ref, image1_ref, image2_ref, projected_ref):
    rows = sums_ref[...]
    a, b, c, d, e = (rows[i : i + 1, :] for i in range(5))
    scale1 = lax.rsqrt(c / count + 1e-06)
    scale1_sq = scale1 * scale1
    alpha = scale1_sq * b / count
    rest_sq = jnp.maximum(scale1_sq * (a - 2.0 * alpha * b + alpha * alpha * c) / count, 0.0)
    scale2 = lax.rsqrt(rest_sq + 1e-06)
    both = scale1 * scale2
    upper = scale1_sq * scale2 * (d - alpha * b) / count
    lower = scale1_sq * scale2 * (a - alpha * b) / count
    corner = both * both * (e - alpha * a - alpha * d + alpha * alpha * b) / count
    projected_ref[...] = jnp.concatenate([alpha, upper, lower, corner, rows[4:8, :] * 0.0], axis=0)
    lanes = h1_ref.shape[1] // rows.shape[1]

    def wide(v):
        return jnp.concatenate([v] * lanes, axis=1)

    h1 = h1_ref[...]
    image1_ref[...] = (h1 * wide(scale1)).astype(image1_ref.dtype)
    image2_ref[...] = ((hh1_ref[...] - wide(alpha) * h1) * wide(both)).astype(image2_ref.dtype)


def on_device(psi, left_env, right_env, left_dims, right_dims, term_shift):
    width = psi.shape[0]
    offsets = jnp.arange(width, dtype=jnp.int32)
    mask_bool = (offsets < left_dims[0])[:, None] & (offsets < right_dims[0])[None, :]
    mask = mask_bool.astype(jnp.float32)
    count = float(lax.axis_size("lsec") * lax.axis_size("rsec") * width * width)
    left_full = lax.all_gather(jnp.transpose(left_env, (1, 0, 2)), "rsec", axis=0, tiled=True)
    right_full = gathered(jnp.transpose(right_env, (2, 0, 1)), "lsec")
    left_full = jnp.transpose(left_full, (1, 0, 2))
    right_full = jnp.transpose(right_full, (1, 2, 0))

    live = jnp.where(mask_bool, psi, jnp.zeros_like(psi))
    live_grid = halo(live)
    h1 = apply_terms(live_grid, left_full, right_full, term_shift, mask)
    h1_grid = halo(h1)
    hh1 = apply_terms(h1_grid, left_full, right_full, term_shift, mask)

    live32 = live.astype(jnp.float32)
    products = jnp.stack([h1 * h1, live32 * h1, live32 * live32, live32 * hh1, h1 * hh1])
    sums = total(jnp.sum(products, axis=(1, 2)))
    rows = jnp.broadcast_to(jnp.pad(sums, (0, 3))[:, None], (8, 128))
    image1, image2, projected_rows = pl.pallas_call(
        functools.partial(tail_kernel, count),
        out_shape=(
            jax.ShapeDtypeStruct(h1.shape, jnp.bfloat16),
            jax.ShapeDtypeStruct(h1.shape, jnp.bfloat16),
            jax.ShapeDtypeStruct((8, 128), jnp.float32),
        ),
    )(rows, h1, hh1)
    projected = projected_rows[:4, 0].reshape(2, 2)
    return (image1, image2, projected)


def solution(mesh):
    in_specs = (
        P("lsec", "rsec"),
        P(None, ("lsec", "rsec"), None),
        P(None, "rsec", "lsec"),
        P("lsec"),
        P("rsec"),
        P(),
    )
    out_specs = (P("lsec", "rsec"), P("lsec", "rsec"), P())
    return jax.shard_map(
        on_device, mesh=mesh, in_specs=in_specs, out_specs=out_specs, check_vma=False
    )
```

```python
import functools

import jax
import jax.numpy as jnp
from jax import lax
from jax.experimental import pallas as pl
from jax.experimental.pallas import tpu as pltpu
from jax.sharding import PartitionSpec as P

AXES = ("lsec", "rsec")


def extended(array, sides, width):
    for axis, dim in sides:
        devices, length = (lax.axis_size(axis), array.shape[dim])
        up = [(i, (i + 1) % devices) for i in range(devices - 1)]
        down = [(j, i) for i, j in up]
        last = lax.slice_in_dim(array, length - width, length, axis=dim)
        leading = lax.slice_in_dim(array, 0, width, axis=dim)
        before = lax.ppermute(last, axis, up)
        after = lax.ppermute(leading, axis, down)
        array = jnp.concatenate([before, array, after], axis=dim)
    return array


def halo(block):
    width = block.shape[0]
    return extended(block.reshape(1, 1, width, width), (("lsec", 0), ("rsec", 1)), 1)


def total(parts):
    devices = lax.axis_size(AXES)
    spread = jnp.broadcast_to(parts[None, :], (devices, parts.shape[0]))
    gathered = lax.all_to_all(spread, AXES, 0, 0, tiled=True)
    return jnp.sum(gathered, axis=0)


def gathered(block, axis):
    devices = lax.axis_size(axis)
    spread = lax.optimization_barrier(jnp.broadcast_to(block[None], (devices,) + block.shape))
    out = lax.all_to_all(spread, axis, 0, 0, tiled=True)
    return out.reshape((devices * block.shape[0],) + block.shape[1:])


def split(x):
    high = x.astype(jnp.bfloat16)
    low = (x - high.astype(jnp.float32)).astype(jnp.bfloat16)
    return high, low


def apply_kernel(shift_ref, grid_ref, left_ref, right_ref, mask_ref, *rest):
    def dot(x, y):
        return jnp.dot(x, y, preferred_element_type=jnp.float32)

    total_ = jnp.zeros(mask_ref.shape, jnp.float32)
    for term in range(left_ref.shape[0]):
        source = grid_ref[1 - shift_ref[term, 0], 1 - shift_ref[term, 1]]
        left = left_ref[term]
        if source.dtype == jnp.bfloat16:
            inner = dot(left, source)
        else:
            high, low = split(source)
            inner = dot(left, high) + dot(left, low)
        high, low = split(inner)
        right = right_ref[term]
        total_ = total_ + (dot(high, right) + dot(low, right))
    if len(rest) == 1:
        rest[0][...] = total_ * mask_ref[...]
        return
    live_ref, out_ref, sums_ref = rest
    hh1 = total_ * mask_ref[...]
    out_ref[...] = hh1
    h1 = grid_ref[1, 1]
    live = live_ref[...].astype(jnp.float32)
    rows = []
    for product in (h1 * h1, live * h1, live * live, live * hh1, h1 * hh1):
        value = jnp.sum(jnp.sum(product, axis=0, keepdims=True), axis=1, keepdims=True)
        rows.append(jnp.broadcast_to(value, (1, sums_ref.shape[1])))
    rows.append(jnp.zeros((sums_ref.shape[0] - 5, sums_ref.shape[1]), jnp.float32))
    sums_ref[...] = jnp.concatenate(rows, axis=0)


def apply_terms(grid, left_env, right_env, term_shift, mask, live=None):
    vmem = pl.BlockSpec(memory_space=pltpu.VMEM)
    smem = pl.BlockSpec(memory_space=pltpu.SMEM)
    image = jax.ShapeDtypeStruct(mask.shape, jnp.float32)
    if live is None:
        return pl.pallas_call(
            apply_kernel, out_shape=image, in_specs=[smem] + [vmem] * 4, out_specs=vmem
        )(term_shift, grid, left_env, right_env, mask)
    return pl.pallas_call(
        apply_kernel,
        out_shape=(image, jax.ShapeDtypeStruct((8, 128), jnp.float32)),
        in_specs=[smem] + [vmem] * 5,
        out_specs=(vmem, vmem),
    )(term_shift, grid, left_env, right_env, mask, live)


def tail_kernel(count, sums_ref, h1_ref, hh1_ref, image1_ref, image2_ref, projected_ref):
    rows = sums_ref[...]
    a, b, c, d, e = (rows[i : i + 1, :] for i in range(5))
    scale1 = lax.rsqrt(c / count + 1e-06)
    scale1_sq = scale1 * scale1
    alpha = scale1_sq * b / count
    rest_sq = jnp.maximum(scale1_sq * (a - 2.0 * alpha * b + alpha * alpha * c) / count, 0.0)
    scale2 = lax.rsqrt(rest_sq + 1e-06)
    both = scale1 * scale2
    upper = scale1_sq * scale2 * (d - alpha * b) / count
    lower = scale1_sq * scale2 * (a - alpha * b) / count
    corner = both * both * (e - alpha * a - alpha * d + alpha * alpha * b) / count
    projected_ref[...] = jnp.concatenate([alpha, upper, lower, corner, rows[4:8, :] * 0.0], axis=0)
    lanes = h1_ref.shape[1] // rows.shape[1]

    def wide(v):
        return jnp.concatenate([v] * lanes, axis=1)

    h1 = h1_ref[...]
    image1_ref[...] = (h1 * wide(scale1)).astype(image1_ref.dtype)
    image2_ref[...] = ((hh1_ref[...] - wide(alpha) * h1) * wide(both)).astype(image2_ref.dtype)


def on_device(psi, left_env, right_env, left_dims, right_dims, term_shift):
    width = psi.shape[0]
    offsets = jnp.arange(width, dtype=jnp.int32)
    mask_bool = (offsets < left_dims[0])[:, None] & (offsets < right_dims[0])[None, :]
    mask = mask_bool.astype(jnp.float32)
    count = float(lax.axis_size("lsec") * lax.axis_size("rsec") * width * width)
    left_full = lax.all_gather(jnp.transpose(left_env, (1, 0, 2)), "rsec", axis=0, tiled=True)
    right_full = gathered(jnp.transpose(right_env, (2, 0, 1)), "lsec")
    left_full = jnp.transpose(left_full, (1, 0, 2))
    right_full = jnp.transpose(right_full, (1, 2, 0))

    live = jnp.where(mask_bool, psi, jnp.zeros_like(psi))
    live_grid = halo(live)
    h1 = apply_terms(live_grid, left_full, right_full, term_shift, mask)
    h1_grid = halo(h1)
    hh1, partial_rows = apply_terms(h1_grid, left_full, right_full, term_shift, mask, live)

    sums = total(partial_rows[:5, 0])
    rows = jnp.broadcast_to(jnp.pad(sums, (0, 3))[:, None], (8, 128))
    image1, image2, projected_rows = pl.pallas_call(
        functools.partial(tail_kernel, count),
        out_shape=(
            jax.ShapeDtypeStruct(h1.shape, jnp.bfloat16),
            jax.ShapeDtypeStruct(h1.shape, jnp.bfloat16),
            jax.ShapeDtypeStruct((8, 128), jnp.float32),
        ),
    )(rows, h1, hh1)
    projected = projected_rows[:4, 0].reshape(2, 2)
    return (image1, image2, projected)


def solution(mesh):
    in_specs = (
        P("lsec", "rsec"),
        P(None, ("lsec", "rsec"), None),
        P(None, "rsec", "lsec"),
        P("lsec"),
        P("rsec"),
        P(),
    )
    out_specs = (P("lsec", "rsec"), P("lsec", "rsec"), P())
    return jax.shard_map(
        on_device, mesh=mesh, in_specs=in_specs, out_specs=out_specs, check_vma=False
    )
```

```python
import functools

import jax
import jax.numpy as jnp
from jax import lax
from jax.experimental import pallas as pl
from jax.experimental.pallas import tpu as pltpu
from jax.sharding import PartitionSpec as P

AXES = ("lsec", "rsec")


def extended(array, sides, width):
    for axis, dim in sides:
        devices, length = (lax.axis_size(axis), array.shape[dim])
        up = [(i, (i + 1) % devices) for i in range(devices - 1)]
        down = [(j, i) for i, j in up]
        last = lax.slice_in_dim(array, length - width, length, axis=dim)
        leading = lax.slice_in_dim(array, 0, width, axis=dim)
        before = lax.ppermute(last, axis, up)
        after = lax.ppermute(leading, axis, down)
        array = jnp.concatenate([before, array, after], axis=dim)
    return array


def halo(block):
    width = block.shape[0]
    return extended(block.reshape(1, 1, width, width), (("lsec", 0), ("rsec", 1)), 1)


def total(parts):
    devices = lax.axis_size(AXES)
    spread = jnp.broadcast_to(parts[None, :], (devices, parts.shape[0]))
    gathered = lax.all_to_all(spread, AXES, 0, 0, tiled=True)
    return jnp.sum(gathered, axis=0)


def gathered(block, axis):
    devices = lax.axis_size(axis)
    spread = lax.optimization_barrier(jnp.broadcast_to(block[None], (devices,) + block.shape))
    out = lax.all_to_all(spread, axis, 0, 0, tiled=True)
    return out.reshape((devices * block.shape[0],) + block.shape[1:])


def split(x):
    high = x.astype(jnp.bfloat16)
    low = (x - high.astype(jnp.float32)).astype(jnp.bfloat16)
    return high, low


def apply_kernel(shift_ref, grid_ref, left_ref, right_ref, mask_ref, *rest):
    def dot(x, y):
        return jnp.dot(x, y, preferred_element_type=jnp.float32)

    total_ = jnp.zeros(mask_ref.shape, jnp.float32)
    for term in range(right_ref.shape[0]):
        source = grid_ref[1 - shift_ref[term, 0], 1 - shift_ref[term, 1]]
        left = jnp.concatenate([left_ref[d, term] for d in range(left_ref.shape[0])], axis=0)
        if source.dtype == jnp.bfloat16:
            inner = dot(left, source)
        else:
            high, low = split(source)
            inner = dot(left, high) + dot(left, low)
        high, low = split(inner)
        right = right_ref[term]
        total_ = total_ + (dot(high, right) + dot(low, right))
    if len(rest) == 1:
        rest[0][...] = total_ * mask_ref[...]
        return
    live_ref, out_ref, sums_ref = rest
    hh1 = total_ * mask_ref[...]
    out_ref[...] = hh1
    h1 = grid_ref[1, 1]
    live = live_ref[...].astype(jnp.float32)
    rows = []
    for product in (h1 * h1, live * h1, live * live, live * hh1, h1 * hh1):
        value = jnp.sum(jnp.sum(product, axis=0, keepdims=True), axis=1, keepdims=True)
        rows.append(jnp.broadcast_to(value, (1, sums_ref.shape[1])))
    rows.append(jnp.zeros((sums_ref.shape[0] - 5, sums_ref.shape[1]), jnp.float32))
    sums_ref[...] = jnp.concatenate(rows, axis=0)


def apply_terms(grid, left_env, right_env, term_shift, mask, live=None):
    vmem = pl.BlockSpec(memory_space=pltpu.VMEM)
    smem = pl.BlockSpec(memory_space=pltpu.SMEM)
    image = jax.ShapeDtypeStruct(mask.shape, jnp.float32)
    if live is None:
        return pl.pallas_call(
            apply_kernel, out_shape=image, in_specs=[smem] + [vmem] * 4, out_specs=vmem
        )(term_shift, grid, left_env, right_env, mask)
    return pl.pallas_call(
        apply_kernel,
        out_shape=(image, jax.ShapeDtypeStruct((8, 128), jnp.float32)),
        in_specs=[smem] + [vmem] * 5,
        out_specs=(vmem, vmem),
    )(term_shift, grid, left_env, right_env, mask, live)


def tail_kernel(count, sums_ref, h1_ref, hh1_ref, image1_ref, image2_ref, projected_ref):
    rows = sums_ref[...]
    a, b, c, d, e = (rows[i : i + 1, :] for i in range(5))
    scale1 = lax.rsqrt(c / count + 1e-06)
    scale1_sq = scale1 * scale1
    alpha = scale1_sq * b / count
    rest_sq = jnp.maximum(scale1_sq * (a - 2.0 * alpha * b + alpha * alpha * c) / count, 0.0)
    scale2 = lax.rsqrt(rest_sq + 1e-06)
    both = scale1 * scale2
    upper = scale1_sq * scale2 * (d - alpha * b) / count
    lower = scale1_sq * scale2 * (a - alpha * b) / count
    corner = both * both * (e - alpha * a - alpha * d + alpha * alpha * b) / count
    projected_ref[...] = jnp.concatenate([alpha, upper, lower, corner, rows[4:8, :] * 0.0], axis=0)
    lanes = h1_ref.shape[1] // rows.shape[1]

    def wide(v):
        return jnp.concatenate([v] * lanes, axis=1)

    h1 = h1_ref[...]
    image1_ref[...] = (h1 * wide(scale1)).astype(image1_ref.dtype)
    image2_ref[...] = ((hh1_ref[...] - wide(alpha) * h1) * wide(both)).astype(image2_ref.dtype)


def on_device(psi, left_env, right_env, left_dims, right_dims, term_shift):
    width = psi.shape[0]
    offsets = jnp.arange(width, dtype=jnp.int32)
    mask_bool = (offsets < left_dims[0])[:, None] & (offsets < right_dims[0])[None, :]
    mask = mask_bool.astype(jnp.float32)
    count = float(lax.axis_size("lsec") * lax.axis_size("rsec") * width * width)
    left_full = lax.all_gather(left_env, "rsec", axis=0, tiled=False)
    right_full = gathered(jnp.transpose(right_env, (2, 0, 1)), "lsec")
    right_full = jnp.transpose(right_full, (1, 2, 0))

    live = jnp.where(mask_bool, psi, jnp.zeros_like(psi))
    live_grid = halo(live)
    h1 = apply_terms(live_grid, left_full, right_full, term_shift, mask)
    h1_grid = halo(h1)
    hh1, partial_rows = apply_terms(h1_grid, left_full, right_full, term_shift, mask, live)

    sums = total(partial_rows[:5, 0])
    rows = jnp.broadcast_to(jnp.pad(sums, (0, 3))[:, None], (8, 128))
    image1, image2, projected_rows = pl.pallas_call(
        functools.partial(tail_kernel, count),
        out_shape=(
            jax.ShapeDtypeStruct(h1.shape, jnp.bfloat16),
            jax.ShapeDtypeStruct(h1.shape, jnp.bfloat16),
            jax.ShapeDtypeStruct((8, 128), jnp.float32),
        ),
    )(rows, h1, hh1)
    projected = projected_rows[:4, 0].reshape(2, 2)
    return (image1, image2, projected)


def solution(mesh):
    in_specs = (
        P("lsec", "rsec"),
        P(None, ("lsec", "rsec"), None),
        P(None, "rsec", "lsec"),
        P("lsec"),
        P("rsec"),
        P(),
    )
    out_specs = (P("lsec", "rsec"), P("lsec", "rsec"), P())
    return jax.shard_map(
        on_device, mesh=mesh, in_specs=in_specs, out_specs=out_specs, check_vma=False
    )
```

```python
import functools

import jax
import jax.numpy as jnp
from jax import lax
from jax.experimental import pallas as pl
from jax.experimental.pallas import tpu as pltpu
from jax.sharding import PartitionSpec as P

AXES = ("lsec", "rsec")


def extended(array, sides, width):
    for axis, dim in sides:
        devices, length = (lax.axis_size(axis), array.shape[dim])
        up = [(i, (i + 1) % devices) for i in range(devices - 1)]
        down = [(j, i) for i, j in up]
        last = lax.slice_in_dim(array, length - width, length, axis=dim)
        leading = lax.slice_in_dim(array, 0, width, axis=dim)
        before = lax.ppermute(last, axis, up)
        after = lax.ppermute(leading, axis, down)
        array = jnp.concatenate([before, array, after], axis=dim)
    return array


def halo(block):
    width = block.shape[0]
    return extended(block.reshape(1, 1, width, width), (("lsec", 0), ("rsec", 1)), 1)


def total(parts):
    devices = lax.axis_size(AXES)
    spread = jnp.broadcast_to(parts[None, :], (devices, parts.shape[0]))
    gathered = lax.all_to_all(spread, AXES, 0, 0, tiled=True)
    return jnp.sum(gathered, axis=0)


def gathered(block, axis):
    devices = lax.axis_size(axis)
    spread = lax.optimization_barrier(jnp.broadcast_to(block[None], (devices,) + block.shape))
    return lax.all_to_all(spread, axis, 0, 0, tiled=True)


def split(x):
    high = x.astype(jnp.bfloat16)
    low = (x - high.astype(jnp.float32)).astype(jnp.bfloat16)
    return high, low


def apply_kernel(shift_ref, grid_ref, left_ref, right_ref, mask_ref, *rest):
    def dot(x, y):
        return jnp.dot(x, y, preferred_element_type=jnp.float32)

    def dot_t(x, y):
        return lax.dot_general(x, y, (((1,), (1,)), ((), ())), preferred_element_type=jnp.float32)

    total_ = jnp.zeros(mask_ref.shape, jnp.float32)
    for term in range(right_ref.shape[1]):
        source = grid_ref[1 - shift_ref[term, 0], 1 - shift_ref[term, 1]]
        left = jnp.concatenate([left_ref[d, term] for d in range(left_ref.shape[0])], axis=0)
        if source.dtype == jnp.bfloat16:
            inner = dot(left, source)
        else:
            high, low = split(source)
            inner = dot(left, high) + dot(left, low)
        high, low = split(inner)
        right = jnp.concatenate([right_ref[d, term] for d in range(right_ref.shape[0])], axis=0)
        total_ = total_ + (dot_t(high, right) + dot_t(low, right))
    if len(rest) == 1:
        rest[0][...] = total_ * mask_ref[...]
        return
    live_ref, out_ref, sums_ref = rest
    hh1 = total_ * mask_ref[...]
    out_ref[...] = hh1
    h1 = grid_ref[1, 1]
    live = live_ref[...].astype(jnp.float32)
    rows = []
    for product in (h1 * h1, live * h1, live * live, live * hh1, h1 * hh1):
        value = jnp.sum(jnp.sum(product, axis=0, keepdims=True), axis=1, keepdims=True)
        rows.append(jnp.broadcast_to(value, (1, sums_ref.shape[1])))
    rows.append(jnp.zeros((sums_ref.shape[0] - 5, sums_ref.shape[1]), jnp.float32))
    sums_ref[...] = jnp.concatenate(rows, axis=0)


def apply_terms(grid, left_env, right_env, term_shift, mask, live=None):
    vmem = pl.BlockSpec(memory_space=pltpu.VMEM)
    smem = pl.BlockSpec(memory_space=pltpu.SMEM)
    image = jax.ShapeDtypeStruct(mask.shape, jnp.float32)
    if live is None:
        return pl.pallas_call(
            apply_kernel, out_shape=image, in_specs=[smem] + [vmem] * 4, out_specs=vmem
        )(term_shift, grid, left_env, right_env, mask)
    return pl.pallas_call(
        apply_kernel,
        out_shape=(image, jax.ShapeDtypeStruct((8, 128), jnp.float32)),
        in_specs=[smem] + [vmem] * 5,
        out_specs=(vmem, vmem),
    )(term_shift, grid, left_env, right_env, mask, live)


def tail_kernel(count, sums_ref, h1_ref, hh1_ref, image1_ref, image2_ref, projected_ref):
    rows = sums_ref[...]
    a, b, c, d, e = (rows[i : i + 1, :] for i in range(5))
    scale1 = lax.rsqrt(c / count + 1e-06)
    scale1_sq = scale1 * scale1
    alpha = scale1_sq * b / count
    rest_sq = jnp.maximum(scale1_sq * (a - 2.0 * alpha * b + alpha * alpha * c) / count, 0.0)
    scale2 = lax.rsqrt(rest_sq + 1e-06)
    both = scale1 * scale2
    upper = scale1_sq * scale2 * (d - alpha * b) / count
    lower = scale1_sq * scale2 * (a - alpha * b) / count
    corner = both * both * (e - alpha * a - alpha * d + alpha * alpha * b) / count
    projected_ref[...] = jnp.concatenate([alpha, upper, lower, corner, rows[4:8, :] * 0.0], axis=0)
    lanes = h1_ref.shape[1] // rows.shape[1]

    def wide(v):
        return jnp.concatenate([v] * lanes, axis=1)

    h1 = h1_ref[...]
    image1_ref[...] = (h1 * wide(scale1)).astype(image1_ref.dtype)
    image2_ref[...] = ((hh1_ref[...] - wide(alpha) * h1) * wide(both)).astype(image2_ref.dtype)


def on_device(psi, left_env, right_env, left_dims, right_dims, term_shift):
    width = psi.shape[0]
    offsets = jnp.arange(width, dtype=jnp.int32)
    mask_bool = (offsets < left_dims[0])[:, None] & (offsets < right_dims[0])[None, :]
    mask = mask_bool.astype(jnp.float32)
    count = float(lax.axis_size("lsec") * lax.axis_size("rsec") * width * width)
    left_full = lax.all_gather(left_env, "rsec", axis=0, tiled=False)
    right_full = gathered(jnp.transpose(right_env, (0, 2, 1)), "lsec")

    live = jnp.where(mask_bool, psi, jnp.zeros_like(psi))
    live_grid = halo(live)
    h1 = apply_terms(live_grid, left_full, right_full, term_shift, mask)
    h1_grid = halo(h1)
    hh1, partial_rows = apply_terms(h1_grid, left_full, right_full, term_shift, mask, live)

    sums = total(partial_rows[:5, 0])
    rows = jnp.broadcast_to(jnp.pad(sums, (0, 3))[:, None], (8, 128))
    image1, image2, projected_rows = pl.pallas_call(
        functools.partial(tail_kernel, count),
        out_shape=(
            jax.ShapeDtypeStruct(h1.shape, jnp.bfloat16),
            jax.ShapeDtypeStruct(h1.shape, jnp.bfloat16),
            jax.ShapeDtypeStruct((8, 128), jnp.float32),
        ),
    )(rows, h1, hh1)
    projected = projected_rows[:4, 0].reshape(2, 2)
    return (image1, image2, projected)


def solution(mesh):
    in_specs = (
        P("lsec", "rsec"),
        P(None, ("lsec", "rsec"), None),
        P(None, "rsec", "lsec"),
        P("lsec"),
        P("rsec"),
        P(),
    )
    out_specs = (P("lsec", "rsec"), P("lsec", "rsec"), P())
    return jax.shard_map(
        on_device, mesh=mesh, in_specs=in_specs, out_specs=out_specs, check_vma=False
    )
```

```python
import functools

import jax
import jax.numpy as jnp
from jax import lax
from jax.experimental import pallas as pl
from jax.experimental.pallas import tpu as pltpu
from jax.sharding import PartitionSpec as P

AXES = ("lsec", "rsec")


def extended(array, sides, width):
    for axis, dim in sides:
        devices, length = (lax.axis_size(axis), array.shape[dim])
        up = [(i, (i + 1) % devices) for i in range(devices - 1)]
        down = [(j, i) for i, j in up]
        last = lax.slice_in_dim(array, length - width, length, axis=dim)
        leading = lax.slice_in_dim(array, 0, width, axis=dim)
        before = lax.ppermute(last, axis, up)
        after = lax.ppermute(leading, axis, down)
        array = jnp.concatenate([before, array, after], axis=dim)
    return array


def halo(block, order=(("lsec", 0), ("rsec", 1))):
    width = block.shape[0]
    return extended(block.reshape(1, 1, width, width), order, 1)


def total(parts):
    devices = lax.axis_size(AXES)
    spread = jnp.broadcast_to(parts[None, :], (devices, parts.shape[0]))
    gathered = lax.all_to_all(spread, AXES, 0, 0, tiled=True)
    return jnp.sum(gathered, axis=0)


def gathered(block, axis):
    devices = lax.axis_size(axis)
    spread = lax.optimization_barrier(jnp.broadcast_to(block[None], (devices,) + block.shape))
    return lax.all_to_all(spread, axis, 0, 0, tiled=True)


def split(x):
    high = x.astype(jnp.bfloat16)
    low = (x - high.astype(jnp.float32)).astype(jnp.bfloat16)
    return high, low


def apply_kernel(shift_ref, grid_ref, left_ref, right_ref, mask_ref, *rest):
    def dot(x, y):
        return jnp.dot(x, y, preferred_element_type=jnp.float32)

    def dot_t(x, y):
        return lax.dot_general(x, y, (((1,), (1,)), ((), ())), preferred_element_type=jnp.float32)

    total_ = jnp.zeros(mask_ref.shape, jnp.float32)
    for term in range(right_ref.shape[1]):
        source = grid_ref[1 - shift_ref[term, 0], 1 - shift_ref[term, 1]]
        left = jnp.concatenate([left_ref[d, term] for d in range(left_ref.shape[0])], axis=0)
        if source.dtype == jnp.bfloat16:
            inner = dot(left, source)
        else:
            high, low = split(source)
            inner = dot(left, high) + dot(left, low)
        high, low = split(inner)
        right = jnp.concatenate([right_ref[d, term] for d in range(right_ref.shape[0])], axis=0)
        total_ = total_ + (dot_t(high, right) + dot_t(low, right))
    if len(rest) == 1:
        rest[0][...] = total_ * mask_ref[...]
        return
    live_ref, out_ref, sums_ref = rest
    hh1 = total_ * mask_ref[...]
    out_ref[...] = hh1
    h1 = grid_ref[1, 1]
    live = live_ref[...].astype(jnp.float32)
    rows = []
    for product in (h1 * h1, live * h1, live * live, live * hh1, h1 * hh1):
        value = jnp.sum(jnp.sum(product, axis=0, keepdims=True), axis=1, keepdims=True)
        rows.append(jnp.broadcast_to(value, (1, sums_ref.shape[1])))
    rows.append(jnp.zeros((sums_ref.shape[0] - 5, sums_ref.shape[1]), jnp.float32))
    sums_ref[...] = jnp.concatenate(rows, axis=0)


def apply_terms(grid, left_env, right_env, term_shift, mask, live=None):
    vmem = pl.BlockSpec(memory_space=pltpu.VMEM)
    smem = pl.BlockSpec(memory_space=pltpu.SMEM)
    image = jax.ShapeDtypeStruct(mask.shape, jnp.float32)
    if live is None:
        return pl.pallas_call(
            apply_kernel, out_shape=image, in_specs=[smem] + [vmem] * 4, out_specs=vmem
        )(term_shift, grid, left_env, right_env, mask)
    return pl.pallas_call(
        apply_kernel,
        out_shape=(image, jax.ShapeDtypeStruct((8, 128), jnp.float32)),
        in_specs=[smem] + [vmem] * 5,
        out_specs=(vmem, vmem),
    )(term_shift, grid, left_env, right_env, mask, live)


def tail_kernel(count, sums_ref, h1_ref, hh1_ref, image1_ref, image2_ref, projected_ref):
    rows = sums_ref[...]
    a, b, c, d, e = (rows[i : i + 1, :] for i in range(5))
    scale1 = lax.rsqrt(c / count + 1e-06)
    scale1_sq = scale1 * scale1
    alpha = scale1_sq * b / count
    rest_sq = jnp.maximum(scale1_sq * (a - 2.0 * alpha * b + alpha * alpha * c) / count, 0.0)
    scale2 = lax.rsqrt(rest_sq + 1e-06)
    both = scale1 * scale2
    upper = scale1_sq * scale2 * (d - alpha * b) / count
    lower = scale1_sq * scale2 * (a - alpha * b) / count
    corner = both * both * (e - alpha * a - alpha * d + alpha * alpha * b) / count
    projected_ref[...] = jnp.concatenate([alpha, upper, lower, corner, rows[4:8, :] * 0.0], axis=0)
    lanes = h1_ref.shape[1] // rows.shape[1]

    def wide(v):
        return jnp.concatenate([v] * lanes, axis=1)

    h1 = h1_ref[...]
    image1_ref[...] = (h1 * wide(scale1)).astype(image1_ref.dtype)
    image2_ref[...] = ((hh1_ref[...] - wide(alpha) * h1) * wide(both)).astype(image2_ref.dtype)


def on_device(psi, left_env, right_env, left_dims, right_dims, term_shift):
    width = psi.shape[0]
    offsets = jnp.arange(width, dtype=jnp.int32)
    mask_bool = (offsets < left_dims[0])[:, None] & (offsets < right_dims[0])[None, :]
    mask = mask_bool.astype(jnp.float32)
    count = float(lax.axis_size("lsec") * lax.axis_size("rsec") * width * width)
    left_full = lax.all_gather(left_env, "rsec", axis=0, tiled=False)
    right_full = gathered(jnp.transpose(right_env, (0, 2, 1)), "lsec")

    live = jnp.where(mask_bool, psi, jnp.zeros_like(psi))
    live_grid = halo(live)
    h1 = apply_terms(live_grid, left_full, right_full, term_shift, mask)
    h1_grid = halo(h1, (("rsec", 1), ("lsec", 0)))
    hh1, partial_rows = apply_terms(h1_grid, left_full, right_full, term_shift, mask, live)

    sums = total(partial_rows[:5, 0])
    rows = jnp.broadcast_to(jnp.pad(sums, (0, 3))[:, None], (8, 128))
    image1, image2, projected_rows = pl.pallas_call(
        functools.partial(tail_kernel, count),
        out_shape=(
            jax.ShapeDtypeStruct(h1.shape, jnp.bfloat16),
            jax.ShapeDtypeStruct(h1.shape, jnp.bfloat16),
            jax.ShapeDtypeStruct((8, 128), jnp.float32),
        ),
    )(rows, h1, hh1)
    projected = projected_rows[:4, 0].reshape(2, 2)
    return (image1, image2, projected)


def solution(mesh):
    in_specs = (
        P("lsec", "rsec"),
        P(None, ("lsec", "rsec"), None),
        P(None, "rsec", "lsec"),
        P("lsec"),
        P("rsec"),
        P(),
    )
    out_specs = (P("lsec", "rsec"), P("lsec", "rsec"), P())
    return jax.shard_map(
        on_device, mesh=mesh, in_specs=in_specs, out_specs=out_specs, check_vma=False
    )
```

```python
import functools

import jax
import jax.numpy as jnp
from jax import lax
from jax.experimental import pallas as pl
from jax.experimental.pallas import tpu as pltpu
from jax.sharding import PartitionSpec as P

AXES = ("lsec", "rsec")


def extended(array, sides, width):
    for axis, dim in sides:
        devices, length = (lax.axis_size(axis), array.shape[dim])
        up = [(i, (i + 1) % devices) for i in range(devices - 1)]
        down = [(j, i) for i, j in up]
        last = lax.slice_in_dim(array, length - width, length, axis=dim)
        leading = lax.slice_in_dim(array, 0, width, axis=dim)
        before = lax.ppermute(last, axis, up)
        after = lax.ppermute(leading, axis, down)
        array = jnp.concatenate([before, array, after], axis=dim)
    return array


def halo(block):
    width = block.shape[0]
    return extended(block.reshape(1, 1, width, width), (("lsec", 0), ("rsec", 1)), 1)


def everyones(parts):
    devices = lax.axis_size(AXES)
    spread = jnp.broadcast_to(parts[None, :], (devices, parts.shape[0]))
    return lax.all_to_all(spread, AXES, 0, 0, tiled=True)


def gathered(block, axis):
    devices = lax.axis_size(axis)
    spread = lax.optimization_barrier(jnp.broadcast_to(block[None], (devices,) + block.shape))
    return lax.all_to_all(spread, axis, 0, 0, tiled=True)


def split(x):
    high = x.astype(jnp.bfloat16)
    low = (x - high.astype(jnp.float32)).astype(jnp.bfloat16)
    return high, low


def apply_kernel(shift_ref, grid_ref, left_ref, right_ref, mask_ref, *rest):
    def dot(x, y):
        return jnp.dot(x, y, preferred_element_type=jnp.float32)

    def dot_t(x, y):
        return lax.dot_general(x, y, (((1,), (1,)), ((), ())), preferred_element_type=jnp.float32)

    total_ = jnp.zeros(mask_ref.shape, jnp.float32)
    for term in range(right_ref.shape[1]):
        source = grid_ref[1 - shift_ref[term, 0], 1 - shift_ref[term, 1]]
        left = jnp.concatenate([left_ref[d, term] for d in range(left_ref.shape[0])], axis=0)
        if source.dtype == jnp.bfloat16:
            inner = dot(left, source)
        else:
            high, low = split(source)
            inner = dot(left, high) + dot(left, low)
        high, low = split(inner)
        right = jnp.concatenate([right_ref[d, term] for d in range(right_ref.shape[0])], axis=0)
        total_ = total_ + (dot_t(high, right) + dot_t(low, right))
    if len(rest) == 1:
        rest[0][...] = total_ * mask_ref[...]
        return
    live_ref, out_ref, sums_ref = rest
    hh1 = total_ * mask_ref[...]
    out_ref[...] = hh1
    h1 = grid_ref[1, 1]
    live = live_ref[...].astype(jnp.float32)
    rows = []
    for product in (h1 * h1, live * h1, live * live, live * hh1, h1 * hh1):
        value = jnp.sum(jnp.sum(product, axis=0, keepdims=True), axis=1, keepdims=True)
        rows.append(jnp.broadcast_to(value, (1, sums_ref.shape[1])))
    rows.append(jnp.zeros((sums_ref.shape[0] - 5, sums_ref.shape[1]), jnp.float32))
    sums_ref[...] = jnp.concatenate(rows, axis=0)


def apply_terms(grid, left_env, right_env, term_shift, mask, live=None):
    vmem = pl.BlockSpec(memory_space=pltpu.VMEM)
    smem = pl.BlockSpec(memory_space=pltpu.SMEM)
    image = jax.ShapeDtypeStruct(mask.shape, jnp.float32)
    if live is None:
        return pl.pallas_call(
            apply_kernel, out_shape=image, in_specs=[smem] + [vmem] * 4, out_specs=vmem
        )(term_shift, grid, left_env, right_env, mask)
    return pl.pallas_call(
        apply_kernel,
        out_shape=(image, jax.ShapeDtypeStruct((8, 128), jnp.float32)),
        in_specs=[smem] + [vmem] * 5,
        out_specs=(vmem, vmem),
    )(term_shift, grid, left_env, right_env, mask, live)


def tail_kernel(count, sums_ref, h1_ref, hh1_ref, image1_ref, image2_ref, projected_ref):
    sums = jnp.sum(sums_ref[...], axis=0, keepdims=True)
    width = projected_ref.shape[1]
    a, b, c, d, e = (jnp.broadcast_to(sums[:, i : i + 1], (1, width)) for i in range(5))
    scale1 = lax.rsqrt(c / count + 1e-06)
    scale1_sq = scale1 * scale1
    alpha = scale1_sq * b / count
    rest_sq = jnp.maximum(scale1_sq * (a - 2.0 * alpha * b + alpha * alpha * c) / count, 0.0)
    scale2 = lax.rsqrt(rest_sq + 1e-06)
    both = scale1 * scale2
    upper = scale1_sq * scale2 * (d - alpha * b) / count
    lower = scale1_sq * scale2 * (a - alpha * b) / count
    corner = both * both * (e - alpha * a - alpha * d + alpha * alpha * b) / count
    spare = jnp.zeros((projected_ref.shape[0] - 4, width), jnp.float32)
    projected_ref[...] = jnp.concatenate([alpha, upper, lower, corner, spare], axis=0)
    lanes = h1_ref.shape[1] // width

    def wide(v):
        return jnp.concatenate([v] * lanes, axis=1)

    h1 = h1_ref[...]
    image1_ref[...] = (h1 * wide(scale1)).astype(image1_ref.dtype)
    image2_ref[...] = ((hh1_ref[...] - wide(alpha) * h1) * wide(both)).astype(image2_ref.dtype)


def on_device(psi, left_env, right_env, left_dims, right_dims, term_shift):
    width = psi.shape[0]
    offsets = jnp.arange(width, dtype=jnp.int32)
    mask_bool = (offsets < left_dims[0])[:, None] & (offsets < right_dims[0])[None, :]
    mask = mask_bool.astype(jnp.float32)
    count = float(lax.axis_size("lsec") * lax.axis_size("rsec") * width * width)
    left_full = lax.all_gather(left_env, "rsec", axis=0, tiled=False)
    right_full = gathered(jnp.transpose(right_env, (0, 2, 1)), "lsec")

    live = jnp.where(mask_bool, psi, jnp.zeros_like(psi))
    live_grid = halo(live)
    h1 = apply_terms(live_grid, left_full, right_full, term_shift, mask)
    h1_grid = halo(h1)
    hh1, partial_rows = apply_terms(h1_grid, left_full, right_full, term_shift, mask, live)

    partials = everyones(partial_rows[:5, 0])
    image1, image2, projected_rows = pl.pallas_call(
        functools.partial(tail_kernel, count),
        out_shape=(
            jax.ShapeDtypeStruct(h1.shape, jnp.bfloat16),
            jax.ShapeDtypeStruct(h1.shape, jnp.bfloat16),
            jax.ShapeDtypeStruct((8, 128), jnp.float32),
        ),
    )(partials, h1, hh1)
    projected = projected_rows[:4, 0].reshape(2, 2)
    return (image1, image2, projected)


def solution(mesh):
    in_specs = (
        P("lsec", "rsec"),
        P(None, ("lsec", "rsec"), None),
        P(None, "rsec", "lsec"),
        P("lsec"),
        P("rsec"),
        P(),
    )
    out_specs = (P("lsec", "rsec"), P("lsec", "rsec"), P())
    return jax.shard_map(
        on_device, mesh=mesh, in_specs=in_specs, out_specs=out_specs, check_vma=False
    )
```
